32 devices in a mesh: dom: 16 (over z, y, x), task: 2 (over core).
Axes of the slice: x: 2, y: 2, z: 4, core: 2. Of those that a mesh axis runs over, the one named last changes fastest.
Arguments:
- positions: float32 [1024, 3, 128], P('dom'), may hold values from 0 to 1
- velocities: float32 [1024, 3, 128], P('dom'), may hold values from -5 to 5
- masses: float32 [1024, 128], P('dom'), may hold values from 0.005 to 0.02
- smoothing: float32 [1024, 128], P('dom'), may hold values from 0.35 to 0.7
- energy: float32 [1024, 128], P('dom'), may hold values from 0.5 to 2
- block_counts: int32 [1024], P('dom'), may hold values from 32 to 128, as said below
- send_lists: int32 [16, 8, 24], P('dom'), may hold values from 0 to 63, as said below
- task_lists: int32 [16, 2, 128], P('dom', 'task'), may hold values from 0 to 16383, as said below
- task_counts: int32 [16, 2], P('dom', 'task'), may hold values from 8 to 128, as said below
Outputs:
- density: float32 [1024, 128], P('dom')
- acceleration: float32 [1024, 3, 128], P('dom')
- energy_rate: float32 [1024, 128], P('dom')
The draws below stay inside these ranges and needn't reach their ends.
Inputs may be any that keep to these rules, and one draw needn't show every extreme that they name: `block_counts`: the valid particles of a block are its first ones; every domain has a full block. `send_lists`: the 24 entries of one domain's list for one direction are different blocks of that domain. `task_lists`: the tasks of a domain (the first task_counts entries of each of its two lists) are all different pairs; entries beyond a list's count are not tasks. `task_counts`: in each domain one of the two devices holds 96 to 128 tasks and the other 8 to 16; which one is drawn.
All inputs are finite; a program needn't handle non-finite values.
Results may differ from the reference program's by a relative error of at most 0.0003.
Values sent between devices are 32-bit elements; how exact they have to be, the bound alone decides.
No kernel may reach another device: no remote copies, remote signals or barrier semaphores. Data moves between devices by JAX's collectives and lax.ppermute only.
A program may use at most 64 MiB of HBM per device.

```python
import math
import jax
import jax.numpy as jnp
from jax import lax

BLOCK_SLOTS = 128
NB = 64
CAP = 128
GY = 8
GH = 24
NS = 256
DOMAINS = 16
BLOCKS = 1024


def draw_block_counts(key, part):
    counts = jax.random.randint(jax.random.fold_in(key, 1), (DOMAINS, NB), BLOCK_SLOTS // 4, BLOCK_SLOTS + 1)
    fullest = jax.random.randint(jax.random.fold_in(key, 2), (DOMAINS, 1), 0, NB)
    counts = jnp.where(jnp.arange(NB)[None, :] == fullest, BLOCK_SLOTS, counts)
    return counts.reshape(BLOCKS).astype(jnp.int32)


def draw_send_lists(key, part):
    keys = jax.random.split(jax.random.fold_in(key, 3), DOMAINS * 8)
    orders = jax.vmap(lambda single: jax.random.permutation(single, NB))(keys)
    return orders[:, :GH].reshape(DOMAINS, 8, GH).astype(jnp.int32)


def task_tables(key):
    keys = jax.random.split(jax.random.fold_in(key, 11), DOMAINS)
    orders = jax.vmap(lambda single: jax.random.permutation(single, NB * NS))(keys).astype(jnp.int32)
    heavy = jax.random.randint(jax.random.fold_in(key, 12), (DOMAINS,), 3 * CAP // 4, CAP + 1)
    light = jax.random.randint(jax.random.fold_in(key, 13), (DOMAINS,), max(CAP // 16, 1), CAP // 8 + 1)
    heavy = heavy.at[0].set(CAP)
    light = light.at[DOMAINS - 1].set(max(CAP // 16, 1))
    which = jax.random.randint(jax.random.fold_in(key, 14), (DOMAINS,), 0, 2)
    first = jnp.where(which == 0, heavy, light).astype(jnp.int32)
    second = jnp.where(which == 0, light, heavy).astype(jnp.int32)
    counts = jnp.stack([first, second], axis=1)
    lists_first = orders[:, :CAP]
    lists_second = jax.vmap(lambda row_order, begin: lax.dynamic_slice_in_dim(row_order, begin, CAP))(orders, first)
    return (jnp.stack([lists_first, lists_second], axis=1).astype(jnp.int32), counts.astype(jnp.int32))


def draw_task_lists(key, part):
    return task_tables(key)[0]


def draw_task_counts(key, part):
    return task_tables(key)[1]


def level_of(stream_key, dims, cuts, least, largest):
    def one(dim, shards_of):
        draws = jax.random.uniform(jax.random.fold_in(jax.random.fold_in(stream_key, 6), dim), (shards_of,), jnp.float32, least / len(cuts), largest / len(cuts))
        return jnp.repeat(jnp.exp(draws), dims[dim] // shards_of).reshape((-1,) + (1,) * (len(dims) - dim - 1))

    loudness = one(*cuts[0])
    for cut in cuts[1:]:
        loudness = loudness * one(*cut)
    return loudness


def gaussian(rng, shape, spread, bound, shards=(), kind=jnp.bfloat16):
    drawn = spread * jax.random.normal(rng, shape, jnp.float32)
    if shards:
        drawn = drawn * level_of(rng, shape, shards, -0.22, 0.18)
    return jnp.clip(drawn, -bound, bound).astype(kind)


def setup_inputs(seed: int = 0) -> dict:
    splits = jax.random.split(jax.random.key(seed), 10)
    positions = jnp.clip(1.0 * jax.random.uniform(splits[0], (BLOCKS, 3, BLOCK_SLOTS), jnp.float32) ** level_of(splits[0], (BLOCKS, 3, BLOCK_SLOTS), ((0, 16),), -0.2, 0.2), 0.0, 1.0)
    velocities = gaussian(splits[1], (BLOCKS, 3, BLOCK_SLOTS), 1.0, 5.0, ((0, 16),), jnp.float32)
    masses = jnp.clip(jnp.exp(math.log(0.02) - 1.3862944 * jax.random.uniform(splits[2], (BLOCKS, BLOCK_SLOTS), jnp.float32) ** level_of(splits[2], (BLOCKS, BLOCK_SLOTS), ((0, 16),), -0.2, 0.2)), 0.005, 0.02)
    smoothing = jnp.clip(jnp.exp(math.log(0.7) - 0.6931472 * jax.random.uniform(splits[3], (BLOCKS, BLOCK_SLOTS), jnp.float32) ** level_of(splits[3], (BLOCKS, BLOCK_SLOTS), ((0, 16),), -0.2, 0.2)), 0.35, 0.7)
    energy = jnp.clip(jnp.exp(math.log(2.0) - 1.3862944 * jax.random.uniform(splits[4], (BLOCKS, BLOCK_SLOTS), jnp.float32) ** level_of(splits[4], (BLOCKS, BLOCK_SLOTS), ((0, 16),), -0.2, 0.2)), 0.5, 2.0)
    block_counts = draw_block_counts(jax.random.fold_in(splits[9], 71), 0)
    send_lists = draw_send_lists(jax.random.fold_in(splits[9], 71), 0)
    task_lists = draw_task_lists(jax.random.fold_in(splits[9], 71), 0)
    task_counts = draw_task_counts(jax.random.fold_in(splits[9], 71), 0)
    return {"positions": positions, "velocities": velocities, "masses": masses, "smoothing": smoothing, "energy": energy, "block_counts": block_counts, "send_lists": send_lists, "task_lists": task_lists, "task_counts": task_counts}


GAMMA = 5.0 / 3.0
VISC_ALPHA = 0.8
KERNEL_NORM = 8.0 / math.pi
DIRECTIONS = ((-1, -1), (-1, 0), (-1, 1), (0, -1), (0, 1), (1, -1), (1, 0), (1, 1))

def spline_value(ratio):
    inner = 1.0 - 6.0 * ratio * ratio + 6.0 * ratio * ratio * ratio
    outer = 2.0 * jnp.maximum(1.0 - ratio, 0.0) ** 3
    return jnp.where(ratio < 0.5, inner, outer)

def spline_slope(ratio):
    inner = -12.0 + 18.0 * ratio
    outer = -6.0 * jnp.maximum(1.0 - ratio, 0.0) ** 2 / jnp.maximum(ratio, 0.5)
    return jnp.where(ratio < 0.5, inner, outer)

def active_flags(source_particle_count, self_block_pair, block_width):
    column = jnp.arange(block_width, dtype=jnp.int32)
    present = column[None, :] < source_particle_count
    distinct = jnp.logical_or(column[:, None] != column[None, :], jnp.logical_not(self_block_pair))
    return jnp.logical_and(present, distinct).astype(jnp.float32)

def geometry(target_feat, source_feat):
    separation = target_feat[0:3, :, None] - source_feat[0:3, None, :]
    dist_sq = lax.optimization_barrier(jnp.sum(separation * separation, axis=0))
    return (separation, dist_sq, jnp.sqrt(dist_sq))

def pair_density(target_feat, source_feat, active_slot):
    separation, dist_sq, radius = geometry(target_feat, source_feat)
    h_target = target_feat[7][:, None]
    kernel = KERNEL_NORM / h_target ** 3 * spline_value(radius / h_target)
    return lax.optimization_barrier(jnp.sum(source_feat[6][None, :] * active_slot * kernel, axis=1))

def pair_force(target_feat, source_feat, active_slot, rho_target, rho_source):
    separation, dist_sq, radius = geometry(target_feat, source_feat)
    h_target = target_feat[7][:, None]
    h_source = source_feat[7][None, :]
    press_target = ((GAMMA - 1.0) * target_feat[8] / rho_target)[:, None]
    press_source = ((GAMMA - 1.0) * source_feat[8] / rho_source)[None, :]
    sound_target = jnp.sqrt(GAMMA * (GAMMA - 1.0) * target_feat[8])[:, None]
    sound_source = jnp.sqrt(GAMMA * (GAMMA - 1.0) * source_feat[8])[None, :]
    slope_target = KERNEL_NORM / h_target ** 5 * spline_slope(radius / h_target)
    slope_source = KERNEL_NORM / h_source ** 5 * spline_slope(radius / h_source)
    approach = lax.optimization_barrier(jnp.sum((target_feat[3:6, :, None] - source_feat[3:6, None, :]) * separation, axis=0))
    h_mean = 0.5 * (h_target + h_source)
    visc_mu = h_mean * jnp.minimum(approach, 0.0) / (dist_sq + 0.01 * h_mean * h_mean)
    rho_mean = 0.5 * (rho_target[:, None] + rho_source[None, :])
    viscosity = (-VISC_ALPHA * 0.5 * (sound_target + sound_source) * visc_mu + 2.0 * VISC_ALPHA * visc_mu * visc_mu) / rho_mean
    weight = source_feat[6][None, :] * active_slot
    slope_mean = 0.5 * (slope_target + slope_source)
    pull = weight * (press_target * slope_target + press_source * slope_source + viscosity * slope_mean)
    accel = -lax.optimization_barrier(jnp.sum(pull[None] * separation, axis=2))
    heating = lax.optimization_barrier(jnp.sum(weight * (press_target * slope_target + 0.5 * viscosity * slope_mean) * approach, axis=1))
    return jnp.concatenate([accel, heating[None]], axis=0)

def reference(positions, velocities, masses, smoothing, energy, block_counts, send_lists, task_lists, task_counts):
    features = jnp.concatenate([positions, velocities, masses[:, None], smoothing[:, None], energy[:, None]], axis=1)
    features = features.reshape(DOMAINS, NB, 9, BLOCK_SLOTS)
    counts = block_counts.reshape(DOMAINS, NB)
    domain_ids = jnp.arange(DOMAINS, dtype=jnp.int32)
    senders = []
    chosen_rows = []
    ghost_feats = []
    ghost_counts = []
    for number, (col_step, row_step) in enumerate(DIRECTIONS):
        sender = ((domain_ids - (col_step * GY + row_step)) % DOMAINS).astype(jnp.int32)
        chosen = send_lists[sender, number].astype(jnp.int32)
        gathered = features[sender[:, None], chosen]
        gathered = jnp.concatenate([gathered[:, :, 0:1] - col_step, gathered[:, :, 1:2] - row_step, gathered[:, :, 2:]], axis=2)
        senders.append(sender)
        chosen_rows.append(chosen)
        ghost_feats.append(gathered)
        ghost_counts.append(counts[sender[:, None], chosen])
    sources = jnp.concatenate([features] + ghost_feats, axis=1)
    source_counts = jnp.concatenate([counts] + ghost_counts, axis=1)
    tasks = task_lists.reshape(DOMAINS, 2 * CAP)
    task_alive = (jnp.arange(CAP, dtype=jnp.int32)[None, None, :] < task_counts[:, :, None]).astype(jnp.float32)
    task_alive = task_alive.reshape(DOMAINS, 2 * CAP)

    def density_domain(inputs):
        domain_feat, region_particle_counts, domain_tasks, domain_alive = inputs

        def one_task(running, item):
            value, living = item
            target_block = value // NS
            source_block = value % NS
            active_slot = active_flags(region_particle_counts[source_block], target_block == source_block, BLOCK_SLOTS)
            term = pair_density(domain_feat[target_block], domain_feat[source_block], active_slot)
            return (running.at[target_block].add(living * term), None)
        result, leftover = lax.scan(one_task, jnp.zeros((NB, BLOCK_SLOTS), jnp.float32), (domain_tasks, domain_alive))
        return result
    rho_sum = lax.map(density_domain, (sources, source_counts, tasks, task_alive))
    rho_own = rho_sum + features[:, :, 6] * KERNEL_NORM / features[:, :, 7] ** 3
    ghost_rho = [rho_own[sender[:, None], chosen] for sender, chosen in zip(senders, chosen_rows)]
    all_rho = jnp.concatenate([rho_own] + ghost_rho, axis=1)

    def force_domain(inputs):
        domain_feat, region_particle_counts, domain_rho, domain_tasks, domain_alive = inputs

        def one_task(running, item):
            value, living = item
            target_block = value // NS
            source_block = value % NS
            active_slot = active_flags(region_particle_counts[source_block], target_block == source_block, BLOCK_SLOTS)
            term = pair_force(domain_feat[target_block], domain_feat[source_block], active_slot, domain_rho[target_block], domain_rho[source_block])
            return (running.at[target_block].add(living * term), None)
        result, leftover = lax.scan(one_task, jnp.zeros((NB, 4, BLOCK_SLOTS), jnp.float32), (domain_tasks, domain_alive))
        return result
    forces = lax.map(force_domain, (sources, source_counts, all_rho, tasks, task_alive))
    valid = jnp.arange(BLOCK_SLOTS, dtype=jnp.int32)[None, None, :] < counts[:, :, None]
    density = jnp.where(valid, rho_own, 0.0).reshape(BLOCKS, BLOCK_SLOTS)
    acceleration = jnp.where(valid[:, :, None, :], forces[:, :, 0:3], 0.0).reshape(BLOCKS, 3, BLOCK_SLOTS)
    energy_rate = jnp.where(valid, forces[:, :, 3], 0.0).reshape(BLOCKS, BLOCK_SLOTS)
    return (density, acceleration, energy_rate)
```

```python
import math

import jax
import jax.numpy as jnp
from jax import lax
from jax.experimental import pallas as pl
from jax.experimental.pallas import tpu as pltpu
from jax.sharding import PartitionSpec as P

GY = 8


GAMMA = 5.0 / 3.0
VISC_ALPHA = 0.8
KERNEL_NORM = 8.0 / math.pi
DIRECTIONS = ((-1, -1), (-1, 0), (-1, 1), (0, -1), (0, 1), (1, -1), (1, 0), (1, 1))
SUB = 8


def passed_along(block, axis, distance):
    devices = range(lax.axis_size(axis))
    route = [((i - distance) % len(devices), i) for i in devices]
    return lax.ppermute(block, axis, route)


def fetch_ghosts(own, send_rows):
    per_direction = send_rows.shape[1]
    picked = jnp.take(own, send_rows.reshape(-1), axis=0, mode="clip")
    picked = picked.reshape((len(DIRECTIONS), per_direction) + own.shape[1:])
    arrived = [
        passed_along(picked[number], "dom", col_step * GY + row_step)
        for number, (col_step, row_step) in enumerate(DIRECTIONS)
    ]
    return jnp.concatenate(arrived, axis=0)


def place_ghosts(ghost_feat, per_direction):
    shifts = []
    for col_step, row_step in DIRECTIONS:
        shifts += [(float(col_step), float(row_step))] * per_direction
    offsets = jnp.asarray(shifts, dtype=ghost_feat.dtype)
    shifted = ghost_feat[:, 0:2, :] - offsets[:, :, None]
    return jnp.concatenate([shifted, ghost_feat[:, 2:, :]], axis=1)


def pick_tasks(task_lists, task_counts):
    both_lists, both_counts = (
        lax.all_gather(task_lists, "task", axis=1, tiled=True),
        lax.all_gather(task_counts, "task", axis=1, tiled=True),
    )
    list_pair = both_lists[0]
    count_pair = both_counts[0]
    capacity = list_pair.shape[1]
    overall = count_pair[0] + count_pair[1]
    member_rank = lax.axis_index("task")
    my_count = (overall + 1 - member_rank) // 2
    places = 2 * jnp.arange(capacity, dtype=jnp.int32) + member_rank
    first_pick = list_pair[0][jnp.clip(places, 0, capacity - 1)]
    second_pick = list_pair[1][jnp.clip(places - count_pair[0], 0, capacity - 1)]
    my_list = jnp.where(places < count_pair[0], first_pick, second_pick)
    return (my_list, my_count)


def spread(row):
    return jnp.broadcast_to(row, (SUB, row.shape[-1]))


def turned(value, tile):
    return pltpu.roll(value, tile * SUB, 1, stride=1, stride_axis=0)


def density_kernel(task_ref, count_ref, feat_ref, out_ref):
    source_total = feat_ref.shape[0]
    lanes = feat_ref.shape[2]
    out_ref[...] = jnp.zeros(out_ref.shape, out_ref.dtype)
    first_row = lax.broadcasted_iota(jnp.int32, (SUB, lanes), 0) == 0

    def one_task(n, carry):
        value = task_ref[n]
        target = value // source_total
        source = value % source_total
        tb = feat_ref[target]
        sb = feat_ref[source]
        xi = spread(tb[0:1])
        yi = spread(tb[1:2])
        zi = spread(tb[2:3])
        hinv = spread(1.0 / tb[7:8])
        xs = spread(sb[0:1])
        ys = spread(sb[1:2])
        zs = spread(sb[2:3])
        ms = spread(sb[6:7])
        acc = jnp.zeros((SUB, lanes), jnp.float32)
        for tile in range(lanes // SUB):
            dx = xi - turned(xs, tile)
            dy = yi - turned(ys, tile)
            dz = zi - turned(zs, tile)
            q = jnp.sqrt(dx * dx + dy * dy + dz * dz) * hinv
            q2 = q * q
            inner = 1.0 + q2 * (6.0 * q - 6.0)
            om = jnp.maximum(1.0 - q, 0.0)
            outer = 2.0 * (om * om * om)
            term = turned(ms, tile) * jnp.where(q < 0.5, inner, outer)
            if tile == 0:
                term = jnp.where(jnp.logical_and(first_row, target == source), 0.0, term)
            acc = acc + term
        out_ref[target] = out_ref[target] + acc
        return carry

    lax.fori_loop(0, count_ref[0], one_task, 0)


def force_rows(block):
    h = block[7:8]
    hinv = 1.0 / h
    h2 = h * h
    g5 = KERNEL_NORM / (h2 * h2 * h)
    energy = block[8:9]
    rho = block[9:10]
    pr = (GAMMA - 1.0) * energy / rho
    half_sound = 0.5 * jnp.sqrt(GAMMA * (GAMMA - 1.0) * energy)
    return dict(
        x=block[0:1], y=block[1:2], z=block[2:3],
        vx=block[3:4], vy=block[4:5], vz=block[5:6],
        m=block[6:7], hh=0.5 * h, hinv=hinv, g5=g5, pr=pr,
        cs=half_sound, rh=0.5 * rho,
    )


def force_kernel(task_ref, count_ref, feat_ref, out_ref):
    source_total = feat_ref.shape[0]
    lanes = feat_ref.shape[2]
    out_ref[...] = jnp.zeros(out_ref.shape, out_ref.dtype)
    first_row = lax.broadcasted_iota(jnp.int32, (SUB, lanes), 0) == 0

    def one_task(n, carry):
        value = task_ref[n]
        target = value // source_total
        source = value % source_total
        ti = {k: spread(v) for k, v in force_rows(feat_ref[target]).items()}
        sj = {k: spread(v) for k, v in force_rows(feat_ref[source]).items()}
        ax = jnp.zeros((SUB, lanes), jnp.float32)
        ay = ax
        az = ax
        heat = ax
        for tile in range(lanes // SUB):
            s = {k: turned(v, tile) for k, v in sj.items()}
            dx = ti["x"] - s["x"]
            dy = ti["y"] - s["y"]
            dz = ti["z"] - s["z"]
            dist_sq = dx * dx + dy * dy + dz * dz
            approach = (ti["vx"] - s["vx"]) * dx + (ti["vy"] - s["vy"]) * dy + (ti["vz"] - s["vz"]) * dz
            radius = jnp.sqrt(dist_sq)
            rinv = 1.0 / radius

            def slope(q, hh):
                om = jnp.maximum(1.0 - q, 0.0)
                return jnp.where(q < 0.5, 18.0 * q - 12.0, (-12.0 * rinv) * (om * om * hh))

            gi = ti["g5"] * slope(radius * ti["hinv"], ti["hh"])
            gj = s["g5"] * slope(radius * s["hinv"], s["hh"])
            hb = ti["hh"] + s["hh"]
            den = dist_sq + 0.01 * (hb * hb)
            lean = hb * jnp.minimum(approach, 0.0)
            sound = ti["cs"] + s["cs"]
            rho_mean = ti["rh"] + s["rh"]
            visc = lean * (2.0 * VISC_ALPHA * lean - VISC_ALPHA * sound * den) / ((den * den) * rho_mean)
            vg = visc * (0.5 * (gi + gj))
            press = ti["pr"] * gi
            weight = s["m"]
            if tile == 0:
                weight = jnp.where(jnp.logical_and(first_row, target == source), 0.0, weight)
            pull = weight * (press + s["pr"] * gj + vg)
            ax = ax + pull * dx
            ay = ay + pull * dy
            az = az + pull * dz
            heat = heat + weight * (press + 0.5 * vg) * approach
        out_ref[target, 0] = out_ref[target, 0] + ax
        out_ref[target, 1] = out_ref[target, 1] + ay
        out_ref[target, 2] = out_ref[target, 2] + az
        out_ref[target, 3] = out_ref[target, 3] + heat
        return carry

    lax.fori_loop(0, count_ref[0], one_task, 0)


def run_kernel(kernel, my_list, my_count, feat, out_shape):
    smem = pl.BlockSpec(memory_space=pltpu.SMEM)
    vmem = pl.BlockSpec(memory_space=pltpu.VMEM)
    return pl.pallas_call(
        kernel,
        out_shape=jax.ShapeDtypeStruct(out_shape, jnp.float32),
        in_specs=[smem, smem, vmem],
        out_specs=vmem,
    )(my_list, jnp.reshape(my_count, (1,)).astype(jnp.int32), feat)


def local(
    positions,
    velocities,
    masses,
    smoothing,
    energy,
    block_counts,
    send_lists,
    task_lists,
    task_counts,
):
    own_count = positions.shape[0]
    block_width = positions.shape[2]
    valid = jnp.arange(block_width, dtype=jnp.int32)[None, :] < block_counts[:, None]
    live_mass = jnp.where(valid, masses, 0.0)
    own_feat = jnp.concatenate(
        [positions, velocities, live_mass[:, None], smoothing[:, None], energy[:, None]], axis=1
    )
    send_rows = send_lists[0]
    ghost_feat = place_ghosts(fetch_ghosts(own_feat, send_rows), send_rows.shape[1])
    all_feat = jnp.concatenate([own_feat, ghost_feat], axis=0)
    my_list, my_count = pick_tasks(task_lists, task_counts)

    partial_rho = run_kernel(
        density_kernel, my_list, my_count, all_feat, (own_count, SUB, block_width)
    )
    partial_rho = KERNEL_NORM / smoothing**3 * jnp.sum(partial_rho, axis=1)
    rho_own = lax.psum(partial_rho, "task") + masses * KERNEL_NORM / smoothing**3
    ghost_rho = fetch_ghosts(rho_own, send_rows)
    all_rho = jnp.concatenate([rho_own, ghost_rho], axis=0)
    force_feat = jnp.concatenate([all_feat, all_rho[:, None]], axis=1)

    partial_force = run_kernel(
        force_kernel, my_list, my_count, force_feat, (own_count, 4, SUB, block_width)
    )
    forces = lax.psum(jnp.sum(partial_force, axis=2), "task")
    density = jnp.where(valid, rho_own, 0.0)
    acceleration = jnp.where(valid[:, None, :], -forces[:, 0:3], 0.0)
    energy_rate = jnp.where(valid, forces[:, 3], 0.0)
    return (density, acceleration, energy_rate)


def solution(mesh):
    placed = (
        P("dom", None, None),
        P("dom", None, None),
        P("dom", None),
        P("dom", None),
        P("dom", None),
        P("dom"),
        P("dom", None, None),
        P("dom", "task", None),
        P("dom", "task"),
    )
    return jax.shard_map(
        local,
        mesh=mesh,
        in_specs=placed,
        out_specs=(P("dom", None), P("dom", None, None), P("dom", None)),
        check_vma=False,
    )
```

```python
import math

import jax
import jax.numpy as jnp
from jax import lax
from jax.experimental import pallas as pl
from jax.experimental.pallas import tpu as pltpu
from jax.sharding import PartitionSpec as P

GY = 8


GAMMA = 5.0 / 3.0
VISC_ALPHA = 0.8
KERNEL_NORM = 8.0 / math.pi
DIRECTIONS = ((-1, -1), (-1, 0), (-1, 1), (0, -1), (0, 1), (1, -1), (1, 0), (1, 1))
SUB = 8


def passed_along(block, axis, distance):
    devices = range(lax.axis_size(axis))
    route = [((i - distance) % len(devices), i) for i in devices]
    return lax.ppermute(block, axis, route)


def fetch_ghosts(own, send_rows):
    per_direction = send_rows.shape[1]
    domains = lax.axis_size("dom")
    picked = jnp.take(own, send_rows.reshape(-1), axis=0, mode="clip")
    picked = picked.reshape((len(DIRECTIONS), per_direction) + own.shape[1:])
    groups = {}
    for number, (col_step, row_step) in enumerate(DIRECTIONS):
        groups.setdefault((col_step * GY + row_step) % domains, []).append(number)
    arrived = [None] * len(DIRECTIONS)
    for distance, members in groups.items():
        payload = jnp.concatenate([picked[number] for number in members], axis=0)
        payload = passed_along(payload, "dom", distance)
        for place, number in enumerate(members):
            arrived[number] = payload[place * per_direction:(place + 1) * per_direction]
    return jnp.concatenate(arrived, axis=0)


def task_sum(partial):
    if lax.axis_size("task") != 2:
        return lax.psum(partial, "task")
    return partial + lax.ppermute(partial, "task", [(0, 1), (1, 0)])


def place_ghosts(ghost_feat, per_direction):
    shifts = []
    for col_step, row_step in DIRECTIONS:
        shifts += [(float(col_step), float(row_step))] * per_direction
    offsets = jnp.asarray(shifts, dtype=ghost_feat.dtype)
    shifted = ghost_feat[:, 0:2, :] - offsets[:, :, None]
    return jnp.concatenate([shifted, ghost_feat[:, 2:, :]], axis=1)


def pick_tasks(task_lists, task_counts):
    mine = jnp.concatenate([task_lists[0, 0], task_counts[0]], axis=0)
    member_rank = lax.axis_index("task")
    if lax.axis_size("task") == 2:
        theirs = lax.ppermute(mine, "task", [(0, 1), (1, 0)])
        first = jnp.where(member_rank == 0, mine, theirs)
        second = jnp.where(member_rank == 0, theirs, mine)
    else:
        both = lax.all_gather(mine, "task", axis=0, tiled=False)
        first, second = both[0], both[1]
    capacity = task_lists.shape[2]
    list_pair = (first[:capacity], second[:capacity])
    count_pair = (first[capacity], second[capacity])
    overall = count_pair[0] + count_pair[1]
    my_count = (overall + 1 - member_rank) // 2
    places = 2 * jnp.arange(capacity, dtype=jnp.int32) + member_rank
    first_pick = list_pair[0][jnp.clip(places, 0, capacity - 1)]
    second_pick = list_pair[1][jnp.clip(places - count_pair[0], 0, capacity - 1)]
    my_list = jnp.where(places < count_pair[0], first_pick, second_pick)
    return (my_list, my_count)


def spread(row):
    return jnp.broadcast_to(row, (SUB, row.shape[-1]))


def turned(value, tile):
    return pltpu.roll(value, tile * SUB, 1, stride=1, stride_axis=0)


def density_kernel(task_ref, count_ref, feat_ref, out_ref):
    source_total = feat_ref.shape[0]
    lanes = feat_ref.shape[2]
    out_ref[...] = jnp.zeros(out_ref.shape, out_ref.dtype)
    first_row = lax.broadcasted_iota(jnp.int32, (SUB, lanes), 0) == 0

    def one_task(n, carry):
        value = task_ref[n]
        target = value // source_total
        source = value % source_total
        tb = feat_ref[target]
        sb = feat_ref[source]
        xi = spread(tb[0:1])
        yi = spread(tb[1:2])
        zi = spread(tb[2:3])
        hinv = spread(1.0 / tb[7:8])
        xs = spread(sb[0:1])
        ys = spread(sb[1:2])
        zs = spread(sb[2:3])
        ms = spread(sb[6:7])
        acc = jnp.zeros((SUB, lanes), jnp.float32)
        for tile in range(lanes // SUB):
            dx = xi - turned(xs, tile)
            dy = yi - turned(ys, tile)
            dz = zi - turned(zs, tile)
            q = jnp.sqrt(dx * dx + dy * dy + dz * dz) * hinv
            q2 = q * q
            inner = 1.0 + q2 * (6.0 * q - 6.0)
            om = jnp.maximum(1.0 - q, 0.0)
            outer = 2.0 * (om * om * om)
            term = turned(ms, tile) * jnp.where(q < 0.5, inner, outer)
            if tile == 0:
                term = jnp.where(jnp.logical_and(first_row, target == source), 0.0, term)
            acc = acc + term
        out_ref[target] = out_ref[target] + acc
        return carry

    lax.fori_loop(0, count_ref[0], one_task, 0)


def force_rows(block):
    h = block[7:8]
    hinv = 1.0 / h
    h2 = h * h
    g5 = KERNEL_NORM / (h2 * h2 * h)
    energy = block[8:9]
    rho = block[9:10]
    pr = (GAMMA - 1.0) * energy / rho
    half_sound = 0.5 * jnp.sqrt(GAMMA * (GAMMA - 1.0) * energy)
    return dict(
        x=block[0:1], y=block[1:2], z=block[2:3],
        vx=block[3:4], vy=block[4:5], vz=block[5:6],
        m=block[6:7], hh=0.5 * h, hinv=hinv, g5=g5, pr=pr,
        cs=half_sound, rh=0.5 * rho,
    )


def force_kernel(task_ref, count_ref, feat_ref, out_ref):
    source_total = feat_ref.shape[0]
    lanes = feat_ref.shape[2]
    out_ref[...] = jnp.zeros(out_ref.shape, out_ref.dtype)
    first_row = lax.broadcasted_iota(jnp.int32, (SUB, lanes), 0) == 0

    def one_task(n, carry):
        value = task_ref[n]
        target = value // source_total
        source = value % source_total
        ti = {k: spread(v) for k, v in force_rows(feat_ref[target]).items()}
        sj = {k: spread(v) for k, v in force_rows(feat_ref[source]).items()}
        ax = jnp.zeros((SUB, lanes), jnp.float32)
        ay = ax
        az = ax
        heat = ax
        for tile in range(lanes // SUB):
            s = {k: turned(v, tile) for k, v in sj.items()}
            dx = ti["x"] - s["x"]
            dy = ti["y"] - s["y"]
            dz = ti["z"] - s["z"]
            dist_sq = dx * dx + dy * dy + dz * dz
            approach = (ti["vx"] - s["vx"]) * dx + (ti["vy"] - s["vy"]) * dy + (ti["vz"] - s["vz"]) * dz
            radius = jnp.sqrt(dist_sq)
            rinv = 1.0 / radius

            def slope(q, hh):
                om = jnp.maximum(1.0 - q, 0.0)
                return jnp.where(q < 0.5, 18.0 * q - 12.0, (-12.0 * rinv) * (om * om * hh))

            gi = ti["g5"] * slope(radius * ti["hinv"], ti["hh"])
            gj = s["g5"] * slope(radius * s["hinv"], s["hh"])
            hb = ti["hh"] + s["hh"]
            den = dist_sq + 0.01 * (hb * hb)
            lean = hb * jnp.minimum(approach, 0.0)
            sound = ti["cs"] + s["cs"]
            rho_mean = ti["rh"] + s["rh"]
            visc = lean * (2.0 * VISC_ALPHA * lean - VISC_ALPHA * sound * den) / ((den * den) * rho_mean)
            vg = visc * (0.5 * (gi + gj))
            press = ti["pr"] * gi
            weight = s["m"]
            if tile == 0:
                weight = jnp.where(jnp.logical_and(first_row, target == source), 0.0, weight)
            pull = weight * (press + s["pr"] * gj + vg)
            ax = ax + pull * dx
            ay = ay + pull * dy
            az = az + pull * dz
            heat = heat + weight * (press + 0.5 * vg) * approach
        out_ref[target, 0] = out_ref[target, 0] + ax
        out_ref[target, 1] = out_ref[target, 1] + ay
        out_ref[target, 2] = out_ref[target, 2] + az
        out_ref[target, 3] = out_ref[target, 3] + heat
        return carry

    lax.fori_loop(0, count_ref[0], one_task, 0)


def run_kernel(kernel, my_list, my_count, feat, out_shape):
    smem = pl.BlockSpec(memory_space=pltpu.SMEM)
    vmem = pl.BlockSpec(memory_space=pltpu.VMEM)
    return pl.pallas_call(
        kernel,
        out_shape=jax.ShapeDtypeStruct(out_shape, jnp.float32),
        in_specs=[smem, smem, vmem],
        out_specs=vmem,
    )(my_list, jnp.reshape(my_count, (1,)).astype(jnp.int32), feat)


def local(
    positions,
    velocities,
    masses,
    smoothing,
    energy,
    block_counts,
    send_lists,
    task_lists,
    task_counts,
):
    own_count = positions.shape[0]
    block_width = positions.shape[2]
    valid = jnp.arange(block_width, dtype=jnp.int32)[None, :] < block_counts[:, None]
    live_mass = jnp.where(valid, masses, 0.0)
    own_feat = jnp.concatenate(
        [positions, velocities, live_mass[:, None], smoothing[:, None], energy[:, None]], axis=1
    )
    send_rows = send_lists[0]
    ghost_feat = place_ghosts(fetch_ghosts(own_feat, send_rows), send_rows.shape[1])
    all_feat = jnp.concatenate([own_feat, ghost_feat], axis=0)
    my_list, my_count = pick_tasks(task_lists, task_counts)

    partial_rho = run_kernel(
        density_kernel, my_list, my_count, all_feat, (own_count, SUB, block_width)
    )
    partial_rho = KERNEL_NORM / smoothing**3 * jnp.sum(partial_rho, axis=1)
    rho_own = task_sum(partial_rho) + masses * KERNEL_NORM / smoothing**3
    ghost_rho = fetch_ghosts(rho_own, send_rows)
    all_rho = jnp.concatenate([rho_own, ghost_rho], axis=0)
    force_feat = jnp.concatenate([all_feat, all_rho[:, None]], axis=1)

    partial_force = run_kernel(
        force_kernel, my_list, my_count, force_feat, (own_count, 4, SUB, block_width)
    )
    forces = task_sum(jnp.sum(partial_force, axis=2))
    density = jnp.where(valid, rho_own, 0.0)
    acceleration = jnp.where(valid[:, None, :], -forces[:, 0:3], 0.0)
    energy_rate = jnp.where(valid, forces[:, 3], 0.0)
    return (density, acceleration, energy_rate)


def solution(mesh):
    placed = (
        P("dom", None, None),
        P("dom", None, None),
        P("dom", None),
        P("dom", None),
        P("dom", None),
        P("dom"),
        P("dom", None, None),
        P("dom", "task", None),
        P("dom", "task"),
    )
    return jax.shard_map(
        local,
        mesh=mesh,
        in_specs=placed,
        out_specs=(P("dom", None), P("dom", None, None), P("dom", None)),
        check_vma=False,
    )
```

```python
import math

import jax
import jax.numpy as jnp
from jax import lax
from jax.experimental import pallas as pl
from jax.experimental.pallas import tpu as pltpu
from jax.sharding import PartitionSpec as P


GY = 8


GAMMA = 5.0 / 3.0
VISC_ALPHA = 0.8
KERNEL_NORM = 8.0 / math.pi
DIRECTIONS = ((-1, -1), (-1, 0), (-1, 1), (0, -1), (0, 1), (1, -1), (1, 0), (1, 1))
SUB = 8


def passed_along(block, axis, distance):
    devices = range(lax.axis_size(axis))
    route = [((i - distance) % len(devices), i) for i in devices]
    return lax.ppermute(block, axis, route)


def fetch_ghosts(own, send_rows):
    per_direction = send_rows.shape[1]
    domains = lax.axis_size("dom")
    picked = jnp.take(own, send_rows.reshape(-1), axis=0, mode="clip")
    picked = picked.reshape((len(DIRECTIONS), per_direction) + own.shape[1:])
    groups = {}
    for number, (col_step, row_step) in enumerate(DIRECTIONS):
        groups.setdefault((col_step * GY + row_step) % domains, []).append(number)
    arrived = [None] * len(DIRECTIONS)
    for distance, members in groups.items():
        payload = jnp.concatenate([picked[number] for number in members], axis=0)
        payload = passed_along(payload, "dom", distance)
        for place, number in enumerate(members):
            arrived[number] = payload[place * per_direction:(place + 1) * per_direction]
    return jnp.concatenate(arrived, axis=0)


def task_sum(partial):
    if lax.axis_size("task") != 2:
        return lax.psum(partial, "task")
    return partial + lax.ppermute(partial, "task", [(0, 1), (1, 0)])


def place_ghosts(ghost_feat, per_direction):
    shifts = []
    for col_step, row_step in DIRECTIONS:
        shifts += [(float(col_step), float(row_step))] * per_direction
    offsets = jnp.asarray(shifts, dtype=ghost_feat.dtype)
    shifted = ghost_feat[:, 0:2, :] - offsets[:, :, None]
    return jnp.concatenate([shifted, ghost_feat[:, 2:, :]], axis=1)


def pick_tasks(task_lists, task_counts):
    mine = jnp.concatenate([task_lists[0, 0], task_counts[0]], axis=0)
    member_rank = lax.axis_index("task")
    if lax.axis_size("task") == 2:
        theirs = lax.ppermute(mine, "task", [(0, 1), (1, 0)])
        first = jnp.where(member_rank == 0, mine, theirs)
        second = jnp.where(member_rank == 0, theirs, mine)
    else:
        both = lax.all_gather(mine, "task", axis=0, tiled=False)
        first, second = both[0], both[1]
    capacity = task_lists.shape[2]
    list_pair = (first[:capacity], second[:capacity])
    count_pair = (first[capacity], second[capacity])
    overall = count_pair[0] + count_pair[1]
    my_count = (overall + 1 - member_rank) // 2
    places = 2 * jnp.arange(capacity, dtype=jnp.int32) + member_rank
    first_pick = list_pair[0][jnp.clip(places, 0, capacity - 1)]
    second_pick = list_pair[1][jnp.clip(places - count_pair[0], 0, capacity - 1)]
    my_list = jnp.where(places < count_pair[0], first_pick, second_pick)
    return (my_list, my_count)


def spread(row):
    return jnp.broadcast_to(row, (SUB, row.shape[-1]))


def turned(value, tile):
    return pltpu.roll(value, tile * SUB, 1, stride=1, stride_axis=0)


def density_kernel(task_ref, count_ref, feat_ref, out_ref):
    source_total = feat_ref.shape[0]
    lanes = feat_ref.shape[2]
    out_ref[...] = jnp.zeros(out_ref.shape, out_ref.dtype)
    first_row = lax.broadcasted_iota(jnp.int32, (SUB, lanes), 0) == 0

    def one_task(n, carry):
        value = task_ref[n]
        target = value // source_total
        source = value % source_total
        tb = feat_ref[target]
        sb = feat_ref[source]
        xi = spread(tb[0:1])
        yi = spread(tb[1:2])
        zi = spread(tb[2:3])
        hinv = spread(1.0 / tb[4:5])
        xs = spread(sb[0:1])
        ys = spread(sb[1:2])
        zs = spread(sb[2:3])
        ms = spread(sb[3:4])
        acc = jnp.zeros((SUB, lanes), jnp.float32)
        for tile in range(lanes // SUB):
            dx = xi - turned(xs, tile)
            dy = yi - turned(ys, tile)
            dz = zi - turned(zs, tile)
            q = jnp.sqrt(dx * dx + dy * dy + dz * dz) * hinv
            q2 = q * q
            inner = 1.0 + q2 * (6.0 * q - 6.0)
            om = jnp.maximum(1.0 - q, 0.0)
            outer = 2.0 * (om * om * om)
            term = turned(ms, tile) * jnp.where(q < 0.5, inner, outer)
            if tile == 0:
                term = jnp.where(jnp.logical_and(first_row, target == source), 0.0, term)
            acc = acc + term
        out_ref[target] = out_ref[target] + acc
        return carry

    lax.fori_loop(0, count_ref[0], one_task, 0)


def force_rows(block):
    h = block[7:8]
    hinv = 1.0 / h
    h2 = h * h
    g5 = KERNEL_NORM / (h2 * h2 * h)
    energy = block[8:9]
    rho = block[9:10]
    pr = (GAMMA - 1.0) * energy / rho
    half_sound = 0.5 * jnp.sqrt(GAMMA * (GAMMA - 1.0) * energy)
    return dict(
        x=block[0:1], y=block[1:2], z=block[2:3],
        vx=block[3:4], vy=block[4:5], vz=block[5:6],
        m=block[6:7], hh=0.5 * h, hinv=hinv, g5=g5, pr=pr,
        cs=half_sound, rh=0.5 * rho,
    )


def force_kernel(task_ref, count_ref, feat_ref, out_ref):
    source_total = feat_ref.shape[0]
    lanes = feat_ref.shape[2]
    out_ref[...] = jnp.zeros(out_ref.shape, out_ref.dtype)
    first_row = lax.broadcasted_iota(jnp.int32, (SUB, lanes), 0) == 0

    def one_task(n, carry):
        value = task_ref[n]
        target = value // source_total
        source = value % source_total
        ti = {k: spread(v) for k, v in force_rows(feat_ref[target]).items()}
        sj = {k: spread(v) for k, v in force_rows(feat_ref[source]).items()}
        ax = jnp.zeros((SUB, lanes), jnp.float32)
        ay = ax
        az = ax
        heat = ax
        for tile in range(lanes // SUB):
            s = {k: turned(v, tile) for k, v in sj.items()}
            dx = ti["x"] - s["x"]
            dy = ti["y"] - s["y"]
            dz = ti["z"] - s["z"]
            dist_sq = dx * dx + dy * dy + dz * dz
            approach = (ti["vx"] - s["vx"]) * dx + (ti["vy"] - s["vy"]) * dy + (ti["vz"] - s["vz"]) * dz
            radius = jnp.sqrt(dist_sq)
            rinv = 1.0 / radius

            def slope(q, hh):
                om = jnp.maximum(1.0 - q, 0.0)
                return jnp.where(q < 0.5, 18.0 * q - 12.0, (-12.0 * rinv) * (om * om * hh))

            gi = ti["g5"] * slope(radius * ti["hinv"], ti["hh"])
            gj = s["g5"] * slope(radius * s["hinv"], s["hh"])
            hb = ti["hh"] + s["hh"]
            den = dist_sq + 0.01 * (hb * hb)
            lean = hb * jnp.minimum(approach, 0.0)
            sound = ti["cs"] + s["cs"]
            rho_mean = ti["rh"] + s["rh"]
            visc = lean * (2.0 * VISC_ALPHA * lean - VISC_ALPHA * sound * den) / ((den * den) * rho_mean)
            vg = visc * (0.5 * (gi + gj))
            press = ti["pr"] * gi
            weight = s["m"]
            if tile == 0:
                weight = jnp.where(jnp.logical_and(first_row, target == source), 0.0, weight)
            pull = weight * (press + s["pr"] * gj + vg)
            ax = ax + pull * dx
            ay = ay + pull * dy
            az = az + pull * dz
            heat = heat + weight * (press + 0.5 * vg) * approach
        out_ref[target, 0] = out_ref[target, 0] + ax
        out_ref[target, 1] = out_ref[target, 1] + ay
        out_ref[target, 2] = out_ref[target, 2] + az
        out_ref[target, 3] = out_ref[target, 3] + heat
        return carry

    lax.fori_loop(0, count_ref[0], one_task, 0)


def run_kernel(kernel, my_list, my_count, feat, out_shape, pair_cost):
    smem = pl.BlockSpec(memory_space=pltpu.SMEM)
    vmem = pl.BlockSpec(memory_space=pltpu.VMEM)
    pairs = my_list.shape[0] * feat.shape[2] * feat.shape[2]
    return pl.pallas_call(
        kernel,
        out_shape=jax.ShapeDtypeStruct(out_shape, jnp.float32),
        in_specs=[smem, smem, vmem],
        out_specs=vmem,
        cost_estimate=pl.CostEstimate(
            flops=pairs * pair_cost, transcendentals=pairs, bytes_accessed=feat.size * 4
        ),
    )(my_list, jnp.reshape(my_count, (1,)).astype(jnp.int32), feat)


def local_body(
    positions,
    velocities,
    masses,
    smoothing,
    energy,
    block_counts,
    send_lists,
    task_lists,
    task_counts,
):
    own_count = positions.shape[0]
    block_width = positions.shape[2]
    valid = jnp.arange(block_width, dtype=jnp.int32)[None, :] < block_counts[:, None]
    live_mass = jnp.where(valid, masses, 0.0)
    send_rows = send_lists[0]
    per_direction = send_rows.shape[1]
    own_near = jnp.concatenate([positions, live_mass[:, None], smoothing[:, None]], axis=1)
    own_move = jnp.concatenate([velocities, energy[:, None]], axis=1)
    ghost_near = place_ghosts(fetch_ghosts(own_near, send_rows), per_direction)
    own_move, ghost_near = lax.optimization_barrier((own_move, ghost_near))
    ghost_move = fetch_ghosts(own_move, send_rows)
    all_near = jnp.concatenate([own_near, ghost_near], axis=0)
    my_list, my_count = pick_tasks(task_lists, task_counts)

    partial_rho = run_kernel(
        density_kernel, my_list, my_count, all_near, (own_count, SUB, block_width), 4096
    )
    partial_rho = KERNEL_NORM / smoothing**3 * jnp.sum(partial_rho, axis=1)
    rho_own = task_sum(partial_rho) + masses * KERNEL_NORM / smoothing**3
    ghost_rho = fetch_ghosts(rho_own, send_rows)
    all_rho = jnp.concatenate([rho_own, ghost_rho], axis=0)
    all_move = jnp.concatenate([own_move, ghost_move], axis=0)
    force_feat = jnp.concatenate(
        [all_near[:, 0:3], all_move[:, 0:3], all_near[:, 3:5], all_move[:, 3:4], all_rho[:, None]],
        axis=1,
    )

    partial_force = run_kernel(
        force_kernel, my_list, my_count, force_feat, (own_count, 4, SUB, block_width), 8192
    )
    forces = task_sum(jnp.sum(partial_force, axis=2))
    density = jnp.where(valid, rho_own, 0.0)
    acceleration = jnp.where(valid[:, None, :], -forces[:, 0:3], 0.0)
    energy_rate = jnp.where(valid, forces[:, 3], 0.0)
    return (density, acceleration, energy_rate)


def solution(mesh):
    placed = (
        P("dom", None, None),
        P("dom", None, None),
        P("dom", None),
        P("dom", None),
        P("dom", None),
        P("dom"),
        P("dom", None, None),
        P("dom", "task", None),
        P("dom", "task"),
    )
    return jax.shard_map(
        local_body,
        mesh=mesh,
        in_specs=placed,
        out_specs=(P("dom", None), P("dom", None, None), P("dom", None)),
        check_vma=False,
    )
```
